512 devices in a mesh: dp: 2 (over core), section: 4 (over x), expert: 64 (over y, z).
Axes of the slice: x: 4, y: 8, z: 8, core: 2. Of those that a mesh axis runs over, the one named last changes fastest.
Arguments:
- grad_out: bfloat16 [16384, 3584], P(('dp', 'expert'), 'section'), may hold values from -6 to 6
- expert_ids: int32 [16384, 8], P(('dp', 'expert')), may hold values from 0 to 63, all different within a row; in each aligned block of 128 rows (0 to 127, 128 to 255, ...) at most 24 rows name the same one
- gate_weights: float32 [16384, 8], P(('dp', 'expert')), may hold values from 0.1 to 1
- act: bfloat16 [16384, 8, 1024], P(('dp', 'expert'), None, 'section'), may hold values from -0.8984375 to 0.8984375
- w_down: bfloat16 [64, 1024, 3584], P('expert', 'section'), may hold values from -0.09375 to 0.09375
Outputs:
- grad_hidden: bfloat16 [16384, 8, 1024], P(('dp', 'expert'), None, 'section')
- grad_gates: float32 [16384, 8], P(('dp', 'expert'))
- grad_w: bfloat16 [64, 1024, 3584], P('expert', 'section', 'dp')
The draws below stay inside these ranges and needn't reach their ends.
Inputs may be any that keep to these rules, and one draw needn't show every extreme that they name: `expert_ids`: each row names 8 different experts. In each aligned block of 128 rows (the tokens of one device) no expert is named by more than 24 rows, and in every draw some expert is named by exactly 24 rows of some block.
All inputs are finite; a program needn't handle non-finite values.
Results may differ from the reference program's by a relative error of at most 0.0058.
Values may be sent and summed in bfloat16 or wider, within the bound.
No kernel may reach another device: no remote copies, remote signals or barrier semaphores. Data moves between devices by JAX's collectives and lax.ppermute only.
A program may use at most 64 MiB of HBM per device.

```python
import math
import jax
import jax.numpy as jnp
import numpy as np
from jax import lax

D = 3584
H = 1024
K = 8
TOK_DEV = 128
EXPERTS = 64
SLOT = 24
ROWS = 1536
TOKENS = 16384
N_DP = 2
N_EXPERT = 64


def block_scale(rng, dims, shards, low, high):
    level, own = 1.0, jax.random.fold_in(rng, 6)
    for dim, shards_of in shards:
        steps = jnp.exp(jax.random.uniform(jax.random.fold_in(own, dim), (shards_of,), jnp.float32, low / len(shards), high / len(shards)))
        level = level * jnp.repeat(steps, dims[dim] // shards_of).reshape([-1 if axis == dim else 1 for axis in range(len(dims))])
    return level


def assign_block(stream_key, own, number, rows, amount, top, limit, lean):
    ranking = jax.random.permutation(stream_key, amount)
    heavy_load, common = shares(amount, rows * top, limit, lean, True), shares(amount, rows * top, limit, lean, False)
    places = jnp.arange(amount)

    def named(sizes, turn):
        used = int((sizes > 0).sum())
        fixed = max(1, used // 4)
        moved = fixed + (places - fixed + turn * (used - fixed)) % max(1, amount - fixed)
        return jnp.zeros((amount,), jnp.int32).at[ranking[jnp.where(places < fixed, places, moved)]].set(jnp.asarray(sizes, jnp.int32))

    sizes = jnp.where(number % 4 == 0, named(heavy_load, number // 4), named(common, number - number // 4 - 1))
    mixed = jax.random.permutation(jax.random.fold_in(own, 3), amount)
    source_of, taker = mixed[0:amount // 2 * 2:2], mixed[1:amount // 2 * 2:2]
    margin = jnp.minimum(sizes[source_of] - 1, limit - sizes[taker]) // 2
    margin = jnp.where((source_of == ranking[0]) | (taker == ranking[0]) | (sizes[taker] == 0), 0, jnp.maximum(margin, 0))
    moved = jax.random.randint(jax.random.fold_in(own, 4), (amount // 2,), 0, 1 << 20) % (margin + 1)
    sizes = sizes.at[source_of].add(-moved).at[taker].add(moved)
    members = jnp.searchsorted(jnp.cumsum(sizes), jnp.arange(rows * top), side="right").astype(jnp.int32)
    listing = members.reshape(top, rows).T
    listing = listing[jax.random.permutation(jax.random.fold_in(own, 1), rows)]
    turn = jax.random.randint(jax.random.fold_in(own, 2), (rows, 1), 0, top)
    return jnp.take_along_axis(listing, (jnp.arange(top)[None, :] + turn) % top, axis=1)


def shares(amount, total, reach, lean, full):
    weights = [(1 << 20) // math.isqrt(rank ** lean) + 1 for rank in range(1, amount + 1)]
    largest = reach if full else min(reach, max(-(-total // amount), total * weights[0] // sum(weights)))
    least = 1 if total - largest >= amount - 1 else 0
    given, surplus = [largest] + [least] * (amount - 1), total - largest - least * (amount - 1)
    while surplus > 0:
        candidates = [i for i in range(1, amount) if given[i] < largest] or [i for i in range(1, amount) if given[i] < reach]
        pool, budget = sum([weights[i] for i in candidates]), surplus
        for i in candidates:
            more = min(reach - given[i], max(1, budget * weights[i] // pool), surplus)
            given[i] = given[i] + more
            surplus = surplus - more
    return np.array(given)


def gaussian(rng, extent, spread, most, pieces=(), kind=jnp.bfloat16):
    result = jax.random.normal(rng, extent, jnp.float32) * spread
    if len(pieces) > 0:
        result = block_scale(rng, extent, pieces, -0.22, 0.18) * result
    return jnp.clip(result, min=-most, max=most).astype(kind)


def setup_inputs(seed: int = 0) -> dict:
    arg_keys = jax.random.split(jax.random.key(seed), 6)
    grad_out = gaussian(arg_keys[0], (TOKENS, D), 1.0, 6.0, ((0, 128), (1, 4)))
    expert_ids_keys = jax.random.split(jax.random.fold_in(arg_keys[1], 1), TOKENS // TOK_DEV)
    expert_ids_turns = jax.random.permutation(jax.random.fold_in(arg_keys[1], 3), TOKENS // TOK_DEV)
    expert_ids = jax.vmap(lambda own, number: assign_block(jax.random.fold_in(arg_keys[1], 2), own, number, TOK_DEV, EXPERTS, K, SLOT, 2))(expert_ids_keys, expert_ids_turns).reshape((TOKENS, K))
    gate_weights = jnp.clip(jnp.exp(math.log(1.0) - 2.3025851 * jax.random.uniform(arg_keys[2], (TOKENS, K), jnp.float32) ** block_scale(arg_keys[2], (TOKENS, K), ((0, 128),), -0.2, 0.2)), 0.1, 1.0)
    act = gaussian(arg_keys[3], (TOKENS, K, H), 0.15, 0.8984375, ((0, 128), (2, 4)))
    w_down = gaussian(arg_keys[4], (EXPERTS, H, D), D ** -0.5, 0.09375, ((0, 64), (1, 4)))
    return {"grad_out": grad_out, "expert_ids": expert_ids, "gate_weights": gate_weights, "act": act, "w_down": w_down}


def reference(grad_out, expert_ids, gate_weights, act, w_down):
    per_replica = TOK_DEV * N_EXPERT
    pair_count = per_replica * K
    scaled = (gate_weights[:, :, None] * act.astype(jnp.float32)).astype(jnp.bfloat16)
    unscaled_parts = []
    weight_total = jnp.zeros((EXPERTS, H, D), jnp.float32)
    for replica in range(N_DP):
        grad_rep = grad_out[replica * per_replica:(replica + 1) * per_replica]
        scaled_rep = scaled[replica * per_replica:(replica + 1) * per_replica]
        targets = expert_ids[replica * per_replica:(replica + 1) * per_replica].reshape(pair_count)
        ordering = jnp.argsort(targets, stable=True).astype(jnp.int32)
        counts = jnp.sum((targets[:, None] == jnp.arange(EXPERTS, dtype=jnp.int32)[None, :]).astype(jnp.int32), axis=0)
        offsets = (jnp.cumsum(counts) - counts).astype(jnp.int32)
        ordering_ext = jnp.concatenate([ordering, jnp.zeros((ROWS,), jnp.int32)])
        chosen_all = ordering_ext[offsets[:, None] + jnp.arange(ROWS, dtype=jnp.int32)[None, :]]
        filled_all = jnp.arange(ROWS, dtype=jnp.int32)[None, :] < counts[:, None]

        def expert_terms(expert):
            chosen = chosen_all[expert]
            filled = filled_all[expert]
            token_at = chosen // K
            route_at = chosen % K
            grad_rows = jnp.where(filled[:, None], grad_rep[token_at], jnp.zeros((), grad_rep.dtype))
            scaled_rows = jnp.where(filled[:, None], scaled_rep[token_at, route_at], jnp.zeros((), scaled_rep.dtype))
            unscaled_rows = jnp.dot(grad_rows, w_down[expert].T, preferred_element_type=jnp.float32)
            weight_part = jnp.dot(scaled_rows.T, grad_rows, preferred_element_type=jnp.float32)
            return unscaled_rows.astype(jnp.bfloat16), weight_part.astype(jnp.bfloat16)

        unscaled_all, weight_parts = lax.map(expert_terms, jnp.arange(EXPERTS, dtype=jnp.int32))
        scatter_at = jnp.where(filled_all, chosen_all, pair_count).reshape(-1)
        unscaled_pairs = jnp.zeros((pair_count, H), jnp.bfloat16).at[scatter_at].set(unscaled_all.reshape(-1, H), mode="drop")
        unscaled_parts.append(unscaled_pairs.reshape(per_replica, K, H))
        weight_total = weight_total + weight_parts.astype(jnp.float32)
    unscaled = jnp.concatenate(unscaled_parts, axis=0)
    grad_hidden = (gate_weights[:, :, None] * unscaled.astype(jnp.float32)).astype(jnp.bfloat16)
    grad_gates = jnp.sum(act.astype(jnp.float32) * unscaled.astype(jnp.float32), axis=2)
    return grad_hidden, grad_gates, weight_total.astype(jnp.bfloat16)
```

```python
import jax
import jax.numpy as jnp
from jax import lax
from jax.sharding import PartitionSpec as P


def routing(expert_ids, experts, capacity):
    tok_count, top_count = expert_ids.shape
    onehot = expert_ids[:, :, None] == jnp.arange(experts, dtype=jnp.int32)[None, None, :]
    per_token = jnp.any(onehot, axis=1).astype(jnp.bfloat16)
    rows = jnp.arange(tok_count, dtype=jnp.int32)
    lower = (rows[:, None] > rows[None, :]).astype(jnp.bfloat16)
    before = jnp.dot(lower, per_token, preferred_element_type=jnp.float32)
    order_in = jnp.sum(jnp.where(onehot, before[:, None, :], 0.0), axis=2).astype(jnp.int32)
    position = expert_ids * capacity + order_in
    slots = jnp.arange(experts * capacity, dtype=jnp.int32)
    sel_pairs = position.reshape(tok_count * top_count)[None, :] == slots[:, None]
    sel_tok = jnp.any(position[None, :, :] == slots[:, None, None], axis=2)
    return sel_pairs.astype(jnp.bfloat16), sel_tok.astype(jnp.bfloat16)


def local(grad_out, expert_ids, gate_weights, act, w_down):
    tok_count, top_count = expert_ids.shape
    hidden_slice = act.shape[2]
    d_slice = grad_out.shape[1]
    n_expert = lax.axis_size("expert")
    n_section = lax.axis_size("section")
    experts = w_down.shape[0] * n_expert
    capacity = 3 * tok_count * top_count // (2 * experts)
    pair_count = tok_count * top_count
    slot_count = experts * capacity

    sel_pairs, sel_tok = routing(expert_ids, experts, capacity)
    scaled = (
        (gate_weights[:, :, None] * act.astype(jnp.float32))
        .astype(jnp.bfloat16)
        .reshape(pair_count, hidden_slice)
    )
    send_scaled = jnp.dot(sel_pairs, scaled, preferred_element_type=jnp.float32).astype(jnp.bfloat16)
    send_grad = jnp.dot(sel_tok, grad_out, preferred_element_type=jnp.float32).astype(jnp.bfloat16)
    send = jnp.concatenate([send_grad, send_scaled], axis=1).reshape(
        experts, capacity, d_slice + hidden_slice
    )
    recv = lax.all_to_all(send, "expert", split_axis=0, concat_axis=0, tiled=True)
    recv = recv.reshape(slot_count, d_slice + hidden_slice)
    recv_grad = recv[:, :d_slice]
    recv_scaled = recv[:, d_slice:]
    spread = jnp.broadcast_to(recv_grad[None], (n_section, slot_count, d_slice))
    gathered = lax.all_to_all(spread, "section", split_axis=0, concat_axis=0, tiled=True)
    w_local = w_down[0].reshape(hidden_slice, n_section, d_slice)
    unscaled = jnp.einsum("srd,hsd->rh", gathered, w_local, preferred_element_type=jnp.float32)
    weight_part = jnp.einsum(
        "rh,srd->hsd", recv_scaled, gathered, preferred_element_type=jnp.float32
    ).astype(jnp.bfloat16).reshape(1, hidden_slice, n_section * d_slice)
    grad_w = lax.psum_scatter(weight_part, "dp", scatter_dimension=2, tiled=True)
    returning = unscaled.astype(jnp.bfloat16).reshape(experts, capacity, hidden_slice)
    returned = lax.all_to_all(returning, "expert", split_axis=0, concat_axis=0, tiled=True)
    unscaled_tok = lax.dot_general(
        sel_pairs,
        returned.reshape(slot_count, hidden_slice),
        (((0,), (0,)), ((), ())),
        preferred_element_type=jnp.float32,
    ).reshape(tok_count, top_count, hidden_slice)
    grad_hidden = (gate_weights[:, :, None] * unscaled_tok).astype(jnp.bfloat16)
    gate_share = jnp.sum(act.astype(jnp.float32) * unscaled_tok, axis=2)
    grad_gates = lax.psum(gate_share, "section")
    return (grad_hidden, grad_gates, grad_w)


def solution(mesh):
    placed = (
        P(("dp", "expert"), "section"),
        P(("dp", "expert"), None),
        P(("dp", "expert"), None),
        P(("dp", "expert"), None, "section"),
        P("expert", "section", None),
    )
    return jax.shard_map(
        local,
        mesh=mesh,
        in_specs=placed,
        out_specs=(
            P(("dp", "expert"), None, "section"),
            P(("dp", "expert"), None),
            P("expert", "section", "dp"),
        ),
        check_vma=False,
    )
```

```python
import jax
import jax.numpy as jnp
from jax import lax
from jax.sharding import PartitionSpec as P


def routing(expert_ids, experts, capacity):
    tok_count, top_count = expert_ids.shape
    onehot = expert_ids[:, :, None] == jnp.arange(experts, dtype=jnp.int32)[None, None, :]
    per_token = jnp.any(onehot, axis=1).astype(jnp.bfloat16)
    rows = jnp.arange(tok_count, dtype=jnp.int32)
    lower = (rows[:, None] > rows[None, :]).astype(jnp.bfloat16)
    before = jnp.dot(lower, per_token, preferred_element_type=jnp.float32)
    order_in = jnp.sum(jnp.where(onehot, before[:, None, :], 0.0), axis=2).astype(jnp.int32)
    position = expert_ids * capacity + order_in
    slots = jnp.arange(experts * capacity, dtype=jnp.int32)
    sel_pairs = position.reshape(tok_count * top_count)[None, :] == slots[:, None]
    sel_tok = jnp.any(position[None, :, :] == slots[:, None, None], axis=2)
    return sel_pairs.astype(jnp.bfloat16), sel_tok.astype(jnp.bfloat16)


def local(grad_out, expert_ids, gate_weights, act, w_down):
    tok_count, top_count = expert_ids.shape
    hidden_slice = act.shape[2]
    d_slice = grad_out.shape[1]
    n_expert = lax.axis_size("expert")
    n_section = lax.axis_size("section")
    experts = w_down.shape[0] * n_expert
    capacity = 3 * tok_count * top_count // (2 * experts)
    pair_count = tok_count * top_count
    slot_count = experts * capacity

    sel_pairs, sel_tok = routing(expert_ids, experts, capacity)
    scaled = (
        (gate_weights[:, :, None] * act.astype(jnp.float32))
        .astype(jnp.bfloat16)
        .reshape(pair_count, hidden_slice)
    )
    send_scaled = jnp.dot(sel_pairs, scaled, preferred_element_type=jnp.float32).astype(jnp.bfloat16)
    send_grad = jnp.dot(sel_tok, grad_out, preferred_element_type=jnp.float32).astype(jnp.bfloat16)
    send = jnp.concatenate([send_grad, send_scaled], axis=1).reshape(
        experts, capacity, d_slice + hidden_slice
    )
    w_local = w_down[0].reshape(hidden_slice, n_section, d_slice)
    chunks = 2
    step = capacity // chunks
    received = []
    for c in range(chunks):
        part = lax.all_to_all(
            send[:, c * step:(c + 1) * step], "expert", split_axis=0, concat_axis=0, tiled=True
        ).reshape(experts * step, d_slice + hidden_slice)
        gathered = lax.all_gather(part[:, :d_slice], "section", axis=0, tiled=False)
        received.append((part[:, d_slice:], gathered))
    weight_acc = None
    returning = []
    for recv_scaled, gathered in received:
        unscaled = jnp.einsum("srd,hsd->rh", gathered, w_local, preferred_element_type=jnp.float32)
        returning.append(unscaled.astype(jnp.bfloat16).reshape(experts, step, hidden_slice))
        term = jnp.einsum("rh,srd->hsd", recv_scaled, gathered, preferred_element_type=jnp.float32)
        weight_acc = term if weight_acc is None else weight_acc + term
    weight_part = weight_acc.astype(jnp.bfloat16).reshape(1, hidden_slice, n_section * d_slice)
    grad_w = lax.psum_scatter(weight_part, "dp", scatter_dimension=2, tiled=True)
    returning = jnp.concatenate(returning, axis=1)
    returned = lax.all_to_all(returning, "expert", split_axis=0, concat_axis=0, tiled=True)
    unscaled_tok = lax.dot_general(
        sel_pairs,
        returned.reshape(slot_count, hidden_slice),
        (((0,), (0,)), ((), ())),
        preferred_element_type=jnp.float32,
    ).reshape(tok_count, top_count, hidden_slice)
    grad_hidden = (gate_weights[:, :, None] * unscaled_tok).astype(jnp.bfloat16)
    gate_share = jnp.sum(act.astype(jnp.float32) * unscaled_tok, axis=2)
    grad_gates = lax.psum(gate_share, "section")
    return (grad_hidden, grad_gates, grad_w)


def solution(mesh):
    placed = (
        P(("dp", "expert"), "section"),
        P(("dp", "expert"), None),
        P(("dp", "expert"), None),
        P(("dp", "expert"), None, "section"),
        P("expert", "section", None),
    )
    return jax.shard_map(
        local,
        mesh=mesh,
        in_specs=placed,
        out_specs=(
            P(("dp", "expert"), None, "section"),
            P(("dp", "expert"), None),
            P("expert", "section", "dp"),
        ),
        check_vma=False,
    )
```

```python
import jax
import jax.numpy as jnp
from jax import lax
from jax.sharding import PartitionSpec as P


def routing(expert_ids, experts, capacity):
    tok_count, top_count = expert_ids.shape
    onehot = expert_ids[:, :, None] == jnp.arange(experts, dtype=jnp.int32)[None, None, :]
    per_token = jnp.any(onehot, axis=1).astype(jnp.bfloat16)
    rows = jnp.arange(tok_count, dtype=jnp.int32)
    lower = (rows[:, None] > rows[None, :]).astype(jnp.bfloat16)
    before = jnp.dot(lower, per_token, preferred_element_type=jnp.float32)
    order_in = jnp.sum(jnp.where(onehot, before[:, None, :], 0.0), axis=2).astype(jnp.int32)
    position = expert_ids * capacity + order_in
    slots = jnp.arange(experts * capacity, dtype=jnp.int32)
    sel_pairs = position.reshape(tok_count * top_count)[None, :] == slots[:, None]
    sel_tok = jnp.any(position[None, :, :] == slots[:, None, None], axis=2)
    return sel_pairs.astype(jnp.bfloat16), sel_tok.astype(jnp.bfloat16)


def local(grad_out, expert_ids, gate_weights, act, w_down):
    tok_count, top_count = expert_ids.shape
    hidden_slice = act.shape[2]
    d_slice = grad_out.shape[1]
    n_expert = lax.axis_size("expert")
    n_section = lax.axis_size("section")
    experts = w_down.shape[0] * n_expert
    capacity = 3 * tok_count * top_count // (2 * experts)
    pair_count = tok_count * top_count
    slot_count = experts * capacity

    sel_pairs, sel_tok = routing(expert_ids, experts, capacity)
    scaled = (
        (gate_weights[:, :, None] * act.astype(jnp.float32))
        .astype(jnp.bfloat16)
        .reshape(pair_count, hidden_slice)
    )
    send_scaled = jnp.dot(sel_pairs, scaled, preferred_element_type=jnp.float32).astype(jnp.bfloat16)
    send_grad = jnp.dot(sel_tok, grad_out, preferred_element_type=jnp.float32).astype(jnp.bfloat16)
    send = jnp.concatenate([send_grad, send_scaled], axis=1).reshape(
        experts, capacity, d_slice + hidden_slice
    )
    section = lax.axis_index("section")
    w_full = lax.all_gather(w_down[0], "section", axis=0, tiled=True)
    w_slice = lax.dynamic_slice_in_dim(w_full, section * d_slice, d_slice, axis=1)
    recv = lax.all_to_all(send, "expert", split_axis=0, concat_axis=0, tiled=True)
    recv = recv.reshape(slot_count, d_slice + hidden_slice)
    recv_grad = recv[:, :d_slice]
    recv_scaled = recv[:, d_slice:]
    scaled_all = lax.all_gather(recv_scaled, "section", axis=0, tiled=False)
    partial = jnp.einsum("rd,hd->rh", recv_grad, w_slice, preferred_element_type=jnp.float32)
    partial = partial.reshape(slot_count, n_section, hidden_slice)
    partial = jnp.transpose(partial, (1, 0, 2))
    pieces = lax.all_to_all(partial, "section", split_axis=0, concat_axis=0, tiled=True)
    unscaled = jnp.sum(pieces, axis=0)
    block = jnp.einsum(
        "srh,rd->shd", scaled_all, recv_grad, preferred_element_type=jnp.float32
    ).astype(jnp.bfloat16)
    blocks = lax.all_to_all(block, "section", split_axis=0, concat_axis=0, tiled=True)
    weight_part = jnp.transpose(blocks, (1, 0, 2)).reshape(1, hidden_slice, n_section * d_slice)
    grad_w = lax.psum_scatter(weight_part, "dp", scatter_dimension=2, tiled=True)
    returning = unscaled.astype(jnp.bfloat16).reshape(experts, capacity, hidden_slice)
    returned = lax.all_to_all(returning, "expert", split_axis=0, concat_axis=0, tiled=True)
    unscaled_tok = lax.dot_general(
        sel_pairs,
        returned.reshape(slot_count, hidden_slice),
        (((0,), (0,)), ((), ())),
        preferred_element_type=jnp.float32,
    ).reshape(tok_count, top_count, hidden_slice)
    grad_hidden = (gate_weights[:, :, None] * unscaled_tok).astype(jnp.bfloat16)
    gate_share = jnp.sum(act.astype(jnp.float32) * unscaled_tok, axis=2)
    grad_gates = lax.psum(gate_share, "section")
    return (grad_hidden, grad_gates, grad_w)


def solution(mesh):
    placed = (
        P(("dp", "expert"), "section"),
        P(("dp", "expert"), None),
        P(("dp", "expert"), None),
        P(("dp", "expert"), None, "section"),
        P("expert", "section", None),
    )

    return jax.shard_map(
        local,
        mesh=mesh,
        in_specs=placed,
        out_specs=(
            P(("dp", "expert"), None, "section"),
            P(("dp", "expert"), None),
            P("expert", "section", "dp"),
        ),
        check_vma=False,
    )
```

```python
import jax
import jax.numpy as jnp
from jax import lax
from jax.sharding import PartitionSpec as P


def routing(expert_ids, experts, capacity):
    tok_count, top_count = expert_ids.shape
    onehot = expert_ids[:, :, None] == jnp.arange(experts, dtype=jnp.int32)[None, None, :]
    per_token = jnp.any(onehot, axis=1).astype(jnp.bfloat16)
    rows = jnp.arange(tok_count, dtype=jnp.int32)
    lower = (rows[:, None] > rows[None, :]).astype(jnp.bfloat16)
    before = jnp.dot(lower, per_token, preferred_element_type=jnp.float32)
    order_in = jnp.sum(jnp.where(onehot, before[:, None, :], 0.0), axis=2).astype(jnp.int32)
    position = expert_ids * capacity + order_in
    slots = jnp.arange(experts * capacity, dtype=jnp.int32)
    sel_pairs = position.reshape(tok_count * top_count)[None, :] == slots[:, None]
    pairs = jnp.arange(tok_count * top_count, dtype=jnp.int32)
    member = (pairs[:, None] // top_count == rows[None, :]).astype(jnp.bfloat16)
    sel_pairs = sel_pairs.astype(jnp.bfloat16)
    sel_tok = jnp.dot(sel_pairs, member, preferred_element_type=jnp.float32).astype(jnp.bfloat16)
    return sel_pairs, sel_tok


def local(grad_out, expert_ids, gate_weights, act, w_down):
    tok_count, top_count = expert_ids.shape
    hidden_slice = act.shape[2]
    d_slice = grad_out.shape[1]
    n_expert = lax.axis_size("expert")
    n_section = lax.axis_size("section")
    experts = w_down.shape[0] * n_expert
    capacity = 3 * tok_count * top_count // (2 * experts)
    pair_count = tok_count * top_count
    slot_count = experts * capacity

    sel_pairs, sel_tok = routing(expert_ids, experts, capacity)
    scaled = (
        (gate_weights[:, :, None] * act.astype(jnp.float32))
        .astype(jnp.bfloat16)
        .reshape(pair_count, hidden_slice)
    )
    send_scaled = jnp.dot(sel_pairs, scaled, preferred_element_type=jnp.float32).astype(jnp.bfloat16)
    send_grad = jnp.dot(sel_tok, grad_out, preferred_element_type=jnp.float32).astype(jnp.bfloat16)
    send = jnp.concatenate([send_grad, send_scaled], axis=1).reshape(
        experts, capacity, d_slice + hidden_slice
    )
    w_local = w_down[0].reshape(hidden_slice, n_section, d_slice)
    recv = lax.all_to_all(send, "expert", split_axis=0, concat_axis=0, tiled=True)
    recv = recv.reshape(slot_count, d_slice + hidden_slice)
    half = slot_count // 2
    first = recv[:half]
    second = recv[half:]
    gathered_first = lax.all_gather(first[:, :d_slice], "section", axis=0, tiled=False)
    spread = jnp.broadcast_to(second[None, :, :d_slice], (n_section, slot_count - half, d_slice))
    gathered_second = lax.all_to_all(spread, "section", split_axis=0, concat_axis=0, tiled=True)
    received = [(first[:, d_slice:], gathered_first), (second[:, d_slice:], gathered_second)]
    weight_acc = None
    returning = []
    for recv_scaled, gathered in received:
        unscaled = jnp.einsum("srd,hsd->rh", gathered, w_local, preferred_element_type=jnp.float32)
        returning.append(unscaled.astype(jnp.bfloat16))
        term = jnp.einsum("rh,srd->hsd", recv_scaled, gathered, preferred_element_type=jnp.float32)
        weight_acc = term if weight_acc is None else weight_acc + term
    weight_part = weight_acc.astype(jnp.bfloat16).reshape(1, hidden_slice, n_section * d_slice)
    grad_w = lax.psum_scatter(weight_part, "dp", scatter_dimension=2, tiled=True)
    returning = jnp.concatenate(returning, axis=0).reshape(experts, capacity, hidden_slice)
    returned = lax.all_to_all(returning, "expert", split_axis=0, concat_axis=0, tiled=True)
    unscaled_tok = lax.dot_general(
        sel_pairs,
        returned.reshape(slot_count, hidden_slice),
        (((0,), (0,)), ((), ())),
        preferred_element_type=jnp.float32,
    ).reshape(tok_count, top_count, hidden_slice)
    grad_hidden = (gate_weights[:, :, None] * unscaled_tok).astype(jnp.bfloat16)
    gate_share = jnp.sum(act.astype(jnp.float32) * unscaled_tok, axis=2)
    grad_gates = lax.psum(gate_share, "section")
    return (grad_hidden, grad_gates, grad_w)


def solution(mesh):
    placed = (
        P(("dp", "expert"), "section"),
        P(("dp", "expert"), None),
        P(("dp", "expert"), None),
        P(("dp", "expert"), None, "section"),
        P("expert", "section", None),
    )
    return jax.shard_map(
        local,
        mesh=mesh,
        in_specs=placed,
        out_specs=(
            P(("dp", "expert"), None, "section"),
            P(("dp", "expert"), None),
            P("expert", "section", "dp"),
        ),
        check_vma=False,
    )
```

```python
import jax
import jax.numpy as jnp
from jax import lax
from jax.sharding import PartitionSpec as P


def routing(expert_ids, experts, capacity):
    tok_count, top_count = expert_ids.shape
    onehot = expert_ids[:, :, None] == jnp.arange(experts, dtype=jnp.int32)[None, None, :]
    per_token = jnp.any(onehot, axis=1).astype(jnp.bfloat16)
    rows = jnp.arange(tok_count, dtype=jnp.int32)
    lower = (rows[:, None] > rows[None, :]).astype(jnp.bfloat16)
    before = jnp.dot(lower, per_token, preferred_element_type=jnp.float32)
    order_in = jnp.sum(jnp.where(onehot, before[:, None, :], 0.0), axis=2).astype(jnp.int32)
    position = expert_ids * capacity + order_in
    slots = jnp.arange(experts * capacity, dtype=jnp.int32)
    sel_pairs = position.reshape(tok_count * top_count)[None, :] == slots[:, None]
    pairs = jnp.arange(tok_count * top_count, dtype=jnp.int32)
    member = (pairs[:, None] // top_count == rows[None, :]).astype(jnp.bfloat16)
    sel_pairs = sel_pairs.astype(jnp.bfloat16)
    sel_tok = jnp.dot(sel_pairs, member, preferred_element_type=jnp.float32).astype(jnp.bfloat16)
    return sel_pairs, sel_tok


def local(grad_out, expert_ids, gate_weights, act, w_down):
    tok_count, top_count = expert_ids.shape
    hidden_slice = act.shape[2]
    d_slice = grad_out.shape[1]
    n_expert = lax.axis_size("expert")
    n_section = lax.axis_size("section")
    experts = w_down.shape[0] * n_expert
    capacity = 3 * tok_count * top_count // (2 * experts)
    pair_count = tok_count * top_count
    slot_count = experts * capacity

    sel_pairs, sel_tok = routing(expert_ids, experts, capacity)
    scaled = (
        (gate_weights[:, :, None] * act.astype(jnp.float32))
        .astype(jnp.bfloat16)
        .reshape(pair_count, hidden_slice)
    )
    send_scaled = jnp.dot(sel_pairs, scaled, preferred_element_type=jnp.float32).astype(jnp.bfloat16)
    send_grad = jnp.dot(sel_tok, grad_out, preferred_element_type=jnp.float32).astype(jnp.bfloat16)
    send = jnp.concatenate([send_grad, send_scaled], axis=1).reshape(
        experts, capacity, d_slice + hidden_slice
    )
    w_local = w_down[0].reshape(hidden_slice, n_section, d_slice)
    chunks = 2
    step = capacity // chunks
    received = []
    for c in range(chunks):
        part = lax.all_to_all(
            send[:, c * step:(c + 1) * step], "expert", split_axis=0, concat_axis=0, tiled=True
        ).reshape(experts * step, d_slice + hidden_slice)
        gathered = lax.all_gather(part[:, :d_slice], "section", axis=0, tiled=False)
        received.append((part[:, d_slice:], gathered))
    weight_acc = None
    returning = []
    for recv_scaled, gathered in received:
        unscaled = jnp.einsum("srd,hsd->rh", gathered, w_local, preferred_element_type=jnp.float32)
        returning.append(unscaled.astype(jnp.bfloat16).reshape(experts, step, hidden_slice))
        term = jnp.einsum("rh,srd->hsd", recv_scaled, gathered, preferred_element_type=jnp.float32)
        weight_acc = term if weight_acc is None else weight_acc + term
    weight_part = weight_acc.astype(jnp.bfloat16).reshape(1, hidden_slice, n_section * d_slice)
    grad_w = lax.psum_scatter(weight_part, "dp", scatter_dimension=2, tiled=True)
    returning = jnp.concatenate(returning, axis=1)
    returned = lax.all_to_all(returning, "expert", split_axis=0, concat_axis=0, tiled=True)
    unscaled_tok = lax.dot_general(
        sel_pairs,
        returned.reshape(slot_count, hidden_slice),
        (((0,), (0,)), ((), ())),
        preferred_element_type=jnp.float32,
    ).reshape(tok_count, top_count, hidden_slice)
    grad_hidden = (gate_weights[:, :, None] * unscaled_tok).astype(jnp.bfloat16)
    gate_share = jnp.sum(act.astype(jnp.float32) * unscaled_tok, axis=2)
    grad_gates = lax.psum(gate_share, "section")
    return (grad_hidden, grad_gates, grad_w)


def solution(mesh):
    placed = (
        P(("dp", "expert"), "section"),
        P(("dp", "expert"), None),
        P(("dp", "expert"), None),
        P(("dp", "expert"), None, "section"),
        P("expert", "section", None),
    )

    return jax.shard_map(
        local,
        mesh=mesh,
        in_specs=placed,
        out_specs=(
            P(("dp", "expert"), None, "section"),
            P(("dp", "expert"), None),
            P("expert", "section", "dp"),
        ),
        check_vma=False,
    )
```

```python
import jax
import jax.numpy as jnp
from jax import lax
from jax.sharding import PartitionSpec as P


def routing(expert_ids, experts, capacity):
    tok_count, top_count = expert_ids.shape
    onehot = expert_ids[:, :, None] == jnp.arange(experts, dtype=jnp.int32)[None, None, :]
    per_token = jnp.any(onehot, axis=1).astype(jnp.bfloat16)
    rows = jnp.arange(tok_count, dtype=jnp.int32)
    lower = (rows[:, None] > rows[None, :]).astype(jnp.bfloat16)
    before = jnp.dot(lower, per_token, preferred_element_type=jnp.float32)
    order_in = jnp.sum(jnp.where(onehot, before[:, None, :], 0.0), axis=2).astype(jnp.int32)
    position = expert_ids * capacity + order_in
    slots = jnp.arange(experts * capacity, dtype=jnp.int32)
    sel_pairs = position.reshape(tok_count * top_count)[None, :] == slots[:, None]
    sel_pairs = sel_pairs.astype(jnp.bfloat16)
    return sel_pairs, position


def local(grad_out, expert_ids, gate_weights, act, w_down):
    tok_count, top_count = expert_ids.shape
    hidden_slice = act.shape[2]
    d_slice = grad_out.shape[1]
    n_expert = lax.axis_size("expert")
    n_section = lax.axis_size("section")
    experts = w_down.shape[0] * n_expert
    capacity = 3 * tok_count * top_count // (2 * experts)
    pair_count = tok_count * top_count
    slot_count = experts * capacity

    sel_pairs, position = routing(expert_ids, experts, capacity)
    scaled = (
        (gate_weights[:, :, None] * act.astype(jnp.float32))
        .astype(jnp.bfloat16)
        .reshape(pair_count, hidden_slice)
    )
    payload = jnp.concatenate(
        [jnp.repeat(grad_out, top_count, axis=0), scaled], axis=1
    )
    flat_pos = position.reshape(pair_count)
    w_local = w_down[0].reshape(hidden_slice, n_section, d_slice)
    chunks = 2
    step = capacity // chunks
    received = []
    for c in range(chunks):
        chunk_slots = (
            jnp.arange(experts, dtype=jnp.int32)[:, None] * capacity
            + c * step
            + jnp.arange(step, dtype=jnp.int32)[None, :]
        ).reshape(experts * step)
        sel_c = (flat_pos[None, :] == chunk_slots[:, None]).astype(jnp.bfloat16)
        send_c = jnp.dot(sel_c, payload, preferred_element_type=jnp.float32).astype(jnp.bfloat16)
        part = lax.all_to_all(
            send_c.reshape(experts, step, d_slice + hidden_slice),
            "expert", split_axis=0, concat_axis=0, tiled=True,
        ).reshape(experts * step, d_slice + hidden_slice)
        gathered = lax.all_gather(part[:, :d_slice], "section", axis=0, tiled=False)
        received.append((part[:, d_slice:], gathered))
    weight_acc = None
    returning = []
    for recv_scaled, gathered in received:
        unscaled = jnp.einsum("srd,hsd->rh", gathered, w_local, preferred_element_type=jnp.float32)
        returning.append(unscaled.astype(jnp.bfloat16).reshape(experts, step, hidden_slice))
        term = jnp.einsum("rh,srd->hsd", recv_scaled, gathered, preferred_element_type=jnp.float32)
        weight_acc = term if weight_acc is None else weight_acc + term
    weight_part = weight_acc.astype(jnp.bfloat16).reshape(1, hidden_slice, n_section * d_slice)
    grad_w = lax.psum_scatter(weight_part, "dp", scatter_dimension=2, tiled=True)
    returning = jnp.concatenate(returning, axis=1)
    returned = lax.all_to_all(returning, "expert", split_axis=0, concat_axis=0, tiled=True)
    unscaled_tok = lax.dot_general(
        sel_pairs,
        returned.reshape(slot_count, hidden_slice),
        (((0,), (0,)), ((), ())),
        preferred_element_type=jnp.float32,
    ).reshape(tok_count, top_count, hidden_slice)
    grad_hidden = (gate_weights[:, :, None] * unscaled_tok).astype(jnp.bfloat16)
    gate_share = jnp.sum(act.astype(jnp.float32) * unscaled_tok, axis=2)
    grad_gates = lax.psum(gate_share, "section")
    return (grad_hidden, grad_gates, grad_w)


def solution(mesh):
    placed = (
        P(("dp", "expert"), "section"),
        P(("dp", "expert"), None),
        P(("dp", "expert"), None),
        P(("dp", "expert"), None, "section"),
        P("expert", "section", None),
    )

    return jax.shard_map(
        local,
        mesh=mesh,
        in_specs=placed,
        out_specs=(
            P(("dp", "expert"), None, "section"),
            P(("dp", "expert"), None),
            P("expert", "section", "dp"),
        ),
        check_vma=False,
    )
```

```python
import jax
import jax.numpy as jnp
from jax import lax
from jax.sharding import PartitionSpec as P


def routing(expert_ids, experts, capacity):
    tok_count, top_count = expert_ids.shape
    onehot = expert_ids[:, :, None] == jnp.arange(experts, dtype=jnp.int32)[None, None, :]
    per_token = jnp.any(onehot, axis=1).astype(jnp.bfloat16)
    rows = jnp.arange(tok_count, dtype=jnp.int32)
    lower = (rows[:, None] > rows[None, :]).astype(jnp.bfloat16)
    before = jnp.dot(lower, per_token, preferred_element_type=jnp.float32)
    order_in = jnp.sum(jnp.where(onehot, before[:, None, :], 0.0), axis=2).astype(jnp.int32)
    position = expert_ids * capacity + order_in
    slots = jnp.arange(experts * capacity, dtype=jnp.int32)
    sel_pairs = position.reshape(tok_count * top_count)[None, :] == slots[:, None]
    sel_pairs = sel_pairs.astype(jnp.bfloat16)
    return sel_pairs, position


def local(grad_out, expert_ids, gate_weights, act, w_down):
    tok_count, top_count = expert_ids.shape
    hidden_slice = act.shape[2]
    d_slice = grad_out.shape[1]
    n_expert = lax.axis_size("expert")
    n_section = lax.axis_size("section")
    experts = w_down.shape[0] * n_expert
    capacity = 3 * tok_count * top_count // (2 * experts)
    pair_count = tok_count * top_count
    slot_count = experts * capacity

    sel_pairs, position = routing(expert_ids, experts, capacity)
    scaled = (
        (gate_weights[:, :, None] * act.astype(jnp.float32))
        .astype(jnp.bfloat16)
        .reshape(pair_count, hidden_slice)
    )
    payload = jnp.concatenate(
        [jnp.repeat(grad_out, top_count, axis=0), scaled], axis=1
    )
    flat_pos = position.reshape(pair_count)
    w_local = w_down[0].reshape(hidden_slice, n_section, d_slice)
    bounds = [(lo, min(lo + 8, capacity)) for lo in range(0, capacity, 8)]
    received = []
    for lo, hi in bounds:
        step = hi - lo
        chunk_slots = (
            jnp.arange(experts, dtype=jnp.int32)[:, None] * capacity
            + lo
            + jnp.arange(step, dtype=jnp.int32)[None, :]
        ).reshape(experts * step)
        sel_c = (flat_pos[None, :] == chunk_slots[:, None]).astype(jnp.bfloat16)
        send_c = jnp.dot(sel_c, payload, preferred_element_type=jnp.float32).astype(jnp.bfloat16)
        part = lax.all_to_all(
            send_c.reshape(experts, step, d_slice + hidden_slice),
            "expert", split_axis=0, concat_axis=0, tiled=True,
        ).reshape(experts * step, d_slice + hidden_slice)
        gathered = lax.all_gather(part[:, :d_slice], "section", axis=0, tiled=False)
        received.append((part[:, d_slice:], gathered, step))
    weight_acc = None
    returning = []
    for recv_scaled, gathered, step in received:
        unscaled = jnp.einsum("srd,hsd->rh", gathered, w_local, preferred_element_type=jnp.float32)
        returning.append(unscaled.astype(jnp.bfloat16).reshape(experts, step, hidden_slice))
        term = jnp.einsum("rh,srd->hsd", recv_scaled, gathered, preferred_element_type=jnp.float32)
        weight_acc = term if weight_acc is None else weight_acc + term
    weight_part = weight_acc.astype(jnp.bfloat16).reshape(1, hidden_slice, n_section * d_slice)
    grad_w = lax.psum_scatter(weight_part, "dp", scatter_dimension=2, tiled=True)
    returning = jnp.concatenate(returning, axis=1)
    returned = lax.all_to_all(returning, "expert", split_axis=0, concat_axis=0, tiled=True)
    unscaled_tok = lax.dot_general(
        sel_pairs,
        returned.reshape(slot_count, hidden_slice),
        (((0,), (0,)), ((), ())),
        preferred_element_type=jnp.float32,
    ).reshape(tok_count, top_count, hidden_slice)
    grad_hidden = (gate_weights[:, :, None] * unscaled_tok).astype(jnp.bfloat16)
    gate_share = jnp.sum(act.astype(jnp.float32) * unscaled_tok, axis=2)
    grad_gates = lax.psum(gate_share, "section")
    return (grad_hidden, grad_gates, grad_w)


def solution(mesh):
    placed = (
        P(("dp", "expert"), "section"),
        P(("dp", "expert"), None),
        P(("dp", "expert"), None),
        P(("dp", "expert"), None, "section"),
        P("expert", "section", None),
    )

    return jax.shard_map(
        local,
        mesh=mesh,
        in_specs=placed,
        out_specs=(
            P(("dp", "expert"), None, "section"),
            P(("dp", "expert"), None),
            P("expert", "section", "dp"),
        ),
        check_vma=False,
    )
```

```python
import jax
import jax.numpy as jnp
from jax import lax
from jax.sharding import PartitionSpec as P


def routing(expert_ids, experts, capacity):
    tok_count, top_count = expert_ids.shape
    onehot = expert_ids[:, :, None] == jnp.arange(experts, dtype=jnp.int32)[None, None, :]
    per_token = jnp.any(onehot, axis=1).astype(jnp.bfloat16)
    rows = jnp.arange(tok_count, dtype=jnp.int32)
    lower = (rows[:, None] > rows[None, :]).astype(jnp.bfloat16)
    before = jnp.dot(lower, per_token, preferred_element_type=jnp.float32)
    order_in = jnp.sum(jnp.where(onehot, before[:, None, :], 0.0), axis=2).astype(jnp.int32)
    position = expert_ids * capacity + order_in
    slots = jnp.arange(experts * capacity, dtype=jnp.int32)
    sel_pairs = position.reshape(tok_count * top_count)[None, :] == slots[:, None]
    sel_pairs = sel_pairs.astype(jnp.bfloat16)
    return sel_pairs, position


def local(grad_out, expert_ids, gate_weights, act, w_down):
    tok_count, top_count = expert_ids.shape
    hidden_slice = act.shape[2]
    d_slice = grad_out.shape[1]
    n_expert = lax.axis_size("expert")
    n_section = lax.axis_size("section")
    experts = w_down.shape[0] * n_expert
    capacity = 3 * tok_count * top_count // (2 * experts)
    pair_count = tok_count * top_count
    slot_count = experts * capacity

    sel_pairs, position = routing(expert_ids, experts, capacity)
    scaled = (
        (gate_weights[:, :, None] * act.astype(jnp.float32))
        .astype(jnp.bfloat16)
        .reshape(pair_count, hidden_slice)
    )
    payload = jnp.concatenate(
        [jnp.repeat(grad_out, top_count, axis=0), scaled], axis=1
    )
    flat_pos = position.reshape(pair_count)
    w_local = w_down[0].reshape(hidden_slice, n_section, d_slice)
    bounds = [(lo, min(lo + 8, capacity)) for lo in range(0, capacity, 8)]
    received = []
    for c, (lo, hi) in enumerate(bounds):
        step = hi - lo
        chunk_slots = (
            jnp.arange(experts, dtype=jnp.int32)[:, None] * capacity
            + lo
            + jnp.arange(step, dtype=jnp.int32)[None, :]
        ).reshape(experts * step)
        sel_c = (flat_pos[None, :] == chunk_slots[:, None]).astype(jnp.bfloat16)
        send_c = jnp.dot(sel_c, payload, preferred_element_type=jnp.float32).astype(jnp.bfloat16)
        part = lax.all_to_all(
            send_c.reshape(experts, step, d_slice + hidden_slice),
            "expert", split_axis=0, concat_axis=0, tiled=True,
        ).reshape(experts * step, d_slice + hidden_slice)
        if c == len(bounds) - 1 and c > 0:
            spread = jnp.broadcast_to(
                part[None, :, :d_slice], (n_section, experts * step, d_slice)
            )
            gathered = lax.all_to_all(spread, "section", split_axis=0, concat_axis=0, tiled=True)
        else:
            gathered = lax.all_gather(part[:, :d_slice], "section", axis=0, tiled=False)
        received.append((part[:, d_slice:], gathered, step))
    weight_acc = None
    returning = []
    for recv_scaled, gathered, step in received:
        unscaled = jnp.einsum("srd,hsd->rh", gathered, w_local, preferred_element_type=jnp.float32)
        returning.append(unscaled.astype(jnp.bfloat16).reshape(experts, step, hidden_slice))
        term = jnp.einsum("rh,srd->hsd", recv_scaled, gathered, preferred_element_type=jnp.float32)
        weight_acc = term if weight_acc is None else weight_acc + term
    weight_part = weight_acc.astype(jnp.bfloat16).reshape(1, hidden_slice, n_section * d_slice)
    grad_w = lax.psum_scatter(weight_part, "dp", scatter_dimension=2, tiled=True)
    returning = jnp.concatenate(returning, axis=1)
    returned = lax.all_to_all(returning, "expert", split_axis=0, concat_axis=0, tiled=True)
    unscaled_tok = lax.dot_general(
        sel_pairs,
        returned.reshape(slot_count, hidden_slice),
        (((0,), (0,)), ((), ())),
        preferred_element_type=jnp.float32,
    ).reshape(tok_count, top_count, hidden_slice)
    grad_hidden = (gate_weights[:, :, None] * unscaled_tok).astype(jnp.bfloat16)
    gate_share = jnp.sum(act.astype(jnp.float32) * unscaled_tok, axis=2)
    grad_gates = lax.psum(gate_share, "section")
    return (grad_hidden, grad_gates, grad_w)


def solution(mesh):
    placed = (
        P(("dp", "expert"), "section"),
        P(("dp", "expert"), None),
        P(("dp", "expert"), None),
        P(("dp", "expert"), None, "section"),
        P("expert", "section", None),
    )

    return jax.shard_map(
        local,
        mesh=mesh,
        in_specs=placed,
        out_specs=(
            P(("dp", "expert"), None, "section"),
            P(("dp", "expert"), None),
            P("expert", "section", "dp"),
        ),
        check_vma=False,
    )
```
